1024 devices in a mesh: seq: 32 (over z, core), enc: 8 (over y), head: 4 (over x).
Axes of the slice: x: 4, y: 8, z: 16, core: 2. Of those that a mesh axis runs over, the one named last changes fastest.
Arguments:
- mel_frames: bfloat16 [65536, 128], P(('seq', 'enc')), may hold values from -6 to 6
- conv_weight: bfloat16 [384, 1280], replicated, may hold values from -0.3125 to 0.3125
- conv_bias: float32 [1280], replicated, may hold values from -3 to 3
- projector: bfloat16 [1280, 8, 1024], P(None, None, 'head'), may hold values from -0.15625 to 0.15625
- seg_offsets: int32 [64], replicated, may hold values from 0 to 65535, as said below
- seg_lengths: int32 [64], replicated, may hold values from 1 to 1535, as said below
- text_embed: bfloat16 [65536, 8192], P('seq', ('enc', 'head')), may hold values from -6 to 6
- mix_taps: float32 [4, 8192], P(None, ('enc', 'head')), may hold values from -3 to 3
- input_map: bfloat16 [65536, 1024], P('seq', 'enc'), may hold values from -1.796875 to 1.796875
- output_map: bfloat16 [65536, 1024], P('seq', 'enc'), may hold values from -1.796875 to 1.796875
- step_size: float32 [128, 65536], P(('enc', 'head'), 'seq'), may hold values from 0 to 2, as said below
- decay_log: float32 [128], P(('enc', 'head')), may hold values from -6 to -2
- skip_gain: float32 [128], P(('enc', 'head')), may hold values from 0.5 to 1.5
Outputs:
- mixer_out: bfloat16 [65536, 8192], P('seq', ('enc', 'head'))
The draws below stay inside these ranges and needn't reach their ends.
Inputs may be any that keep to these rules, and one draw needn't show every extreme that they name: `seg_offsets`: offsets rise; owner k's two segments lie within positions k * 2048 to (k+1) * 2048 - 1 without intersection. Owner k's audio tokens are those of track indices within 256 of k * 1024 to (k+1) * 1024 - 1; in every draw some owner takes 256 tokens from each neighbour's share. `seg_lengths`: the lengths sum to 32768; an owner's two segments together hold between 512 and 1536 tokens. `step_size`: Positive.
All inputs are finite; a program needn't handle non-finite values.
Results may differ from the reference program's by a relative error of at most 0.006.
Values may be sent and summed in bfloat16 or wider, within the bound.
No kernel may reach another device: no remote copies, remote signals or barrier semaphores. Data moves between devices by JAX's collectives and lax.ppermute only.
A program may use at most 64 MiB of HBM per device.

```python
import math
import jax
import jax.numpy as jnp
from jax import lax

MEL = 128
ENC_W = 1280
HDIM = 64
STATE = 128
SPAN = 128
L_DEV = 2048
HEADS = 128
INNER = 8192
GROUPS = 8
OWNERS = 32
SEQ_LEN = 65536
AUD_DEV = 1024
AUD = 32768
DRIFT = 256
N_ENC = 8


def layout(key):
    base_key = jax.random.fold_in(key, 7)
    drift_key = jax.random.fold_in(base_key, 1)
    first_key = jax.random.fold_in(base_key, 2)
    split_key = jax.random.fold_in(base_key, 4)
    inner_drift = jax.random.randint(drift_key, (OWNERS - 1,), -DRIFT, DRIFT + 1)
    big_owner = jax.random.randint(first_key, (), 1, OWNERS - 1)
    indices = jnp.arange(OWNERS - 1, dtype=jnp.int32)
    inner_drift = jnp.where(indices == big_owner, DRIFT, jnp.where(indices == big_owner - 1, -DRIFT, inner_drift))
    zero_one = jnp.zeros((1,), jnp.int32)
    drift_all = jnp.concatenate([zero_one, inner_drift.astype(jnp.int32), zero_one])
    audio_counts = AUD_DEV + drift_all[1:] - drift_all[:-1]
    text_counts = L_DEV - audio_counts
    raw_draws = jax.random.randint(split_key, (OWNERS, 3), 0, 1 << 20)
    owner_ids = jnp.arange(OWNERS, dtype=jnp.int32)
    is_last = owner_ids == OWNERS - 1
    forced = (owner_ids == big_owner) | is_last
    first_length = jnp.where(forced, audio_counts - 1, jnp.remainder(raw_draws[:, 0], audio_counts - 1) + 1)
    cut_one = jnp.remainder(raw_draws[:, 1], text_counts + 1)
    cut_two = jnp.where(is_last, text_counts, jnp.remainder(raw_draws[:, 2], text_counts + 1))
    low_cut = jnp.minimum(cut_one, cut_two)
    high_cut = jnp.maximum(cut_one, cut_two)
    block_base = owner_ids * L_DEV
    offset_first = block_base + low_cut
    offset_second = block_base + high_cut + first_length
    offsets = jnp.stack([offset_first, offset_second], axis=1).reshape(-1).astype(jnp.int32)
    lengths = jnp.stack([first_length, audio_counts - first_length], axis=1).reshape(-1).astype(jnp.int32)
    return (offsets, lengths)


def draw_seg_offsets(key, part):
    return layout(key)[0]


def draw_seg_lengths(key, part):
    return layout(key)[1]


def slow_heads(key):
    head_key = jax.random.fold_in(key, 11)
    share = 0.5
    return jax.random.uniform(head_key, (HEADS,), jnp.float32) < share


def draw_step_size(key, part):
    slow = slow_heads(key)
    rough_key = jax.random.fold_in(key, 23)
    owner_key = jax.random.fold_in(key, 29)
    rough = jnp.exp(jax.random.uniform(rough_key, (HEADS, SEQ_LEN), jnp.float32, math.log(0.5), math.log(2.0)))
    owner_scale = jnp.exp(jax.random.uniform(owner_key, (OWNERS,), jnp.float32, math.log(0.7), math.log(1.4)))
    per_place = jnp.repeat(owner_scale, L_DEV)
    head_scale = jnp.where(slow, 0.002, 0.5)
    return (head_scale[:, None] * rough * per_place[None, :]).astype(jnp.float32)


def draw_decay_log(key, part):
    slow = slow_heads(key)
    rate_key = jax.random.fold_in(key, 31)
    spread = jax.random.uniform(rate_key, (HEADS,), jnp.float32)
    slow_rate = math.log(0.003) + spread * (math.log(0.01) - math.log(0.003))
    fast_rate = math.log(0.03) + spread * (math.log(0.1) - math.log(0.03))
    return jnp.where(slow, slow_rate, fast_rate).astype(jnp.float32)


def level_of(rng, extent, pieces, low, top_value):
    loudness = 1.0
    for position, blocks in pieces:
        steps = jax.random.uniform(jax.random.fold_in(jax.random.fold_in(rng, 6), position), (blocks,), jnp.float32, low / len(pieces), top_value / len(pieces))
        loudness = loudness * jnp.repeat(jnp.exp(steps), extent[position] // blocks).reshape((-1,) + (1,) * (len(extent) - 1 - position))
    return loudness


def centred(stream_key, dims, scale, limit, shards=(), kind=jnp.bfloat16):
    values = jax.random.normal(stream_key, dims, jnp.float32) * scale
    if len(shards) > 0:
        values = level_of(stream_key, dims, shards, -0.22, 0.18) * values
    return jnp.clip(values, min=-limit, max=limit).astype(kind)


def setup_inputs(seed: int = 0) -> dict:
    key_list = jax.random.split(jax.random.key(seed), 14)
    mel_frames = centred(key_list[0], (2 * AUD, MEL), 1.0, 6.0, ((0, 256),))
    conv_weight = centred(key_list[1], (3 * MEL, ENC_W), (3 * MEL) ** -0.5, 0.3125)
    conv_bias = centred(key_list[2], (ENC_W,), 0.5, 3.0, (), jnp.float32)
    projector = centred(key_list[3], (ENC_W, N_ENC, INNER // N_ENC), ENC_W ** -0.5, 0.15625, ((2, 4),))
    seg_offsets = draw_seg_offsets(jax.random.fold_in(key_list[13], 71), 0)
    seg_lengths = draw_seg_lengths(jax.random.fold_in(key_list[13], 71), 0)
    text_embed = centred(key_list[6], (SEQ_LEN, INNER), 1.0, 6.0, ((0, 32), (1, 32)))
    mix_taps = centred(key_list[7], (4, INNER), 4 ** -0.5, 3.0, ((1, 32),), jnp.float32)
    input_map = centred(key_list[8], (SEQ_LEN, GROUPS * STATE), 0.3, 1.796875, ((0, 32), (1, 8)))
    output_map = centred(key_list[9], (SEQ_LEN, GROUPS * STATE), 0.3, 1.796875, ((0, 32), (1, 8)))
    step_size = draw_step_size(jax.random.fold_in(key_list[13], 71), 0)
    decay_log = draw_decay_log(jax.random.fold_in(key_list[13], 71), 0)
    skip_gain = jnp.clip(0.5 + 1.0 * jax.random.uniform(key_list[12], (HEADS,), jnp.float32) ** level_of(key_list[12], (HEADS,), ((0, 32),), -0.2, 0.2), 0.5, 1.5)
    return {"mel_frames": mel_frames, "conv_weight": conv_weight, "conv_bias": conv_bias, "projector": projector, "seg_offsets": seg_offsets, "seg_lengths": seg_lengths, "text_embed": text_embed, "mix_taps": mix_taps, "input_map": input_map, "output_map": output_map, "step_size": step_size, "decay_log": decay_log, "skip_gain": skip_gain}


highest = lax.Precision.HIGHEST
high_mode = lax.Precision.HIGH


def front_end(mel_frames, conv_weight, conv_bias, seg_lengths):
    seg_start = jnp.cumsum(seg_lengths) - seg_lengths
    frame_pairs = mel_frames.reshape(AUD, 2 * MEL)
    tokens = jnp.arange(AUD, dtype=jnp.int32)
    opening = jnp.any(tokens[:, None] == seg_start[None, :], axis=1)
    left_frames = jnp.concatenate([jnp.zeros((1, MEL), mel_frames.dtype), frame_pairs[:-1, MEL:]], axis=0)
    left_frames = jnp.where(opening[:, None], jnp.zeros_like(left_frames), left_frames)
    stacked = jnp.concatenate([left_frames, frame_pairs], axis=1)
    summed = jnp.dot(stacked, conv_weight, preferred_element_type=jnp.float32) + conv_bias
    return jax.nn.gelu(summed, approximate=False).astype(jnp.bfloat16)


def place_tokens(audio, text_embed, seg_offsets, seg_lengths):
    seg_start = jnp.cumsum(seg_lengths) - seg_lengths
    places = jnp.arange(SEQ_LEN, dtype=jnp.int32)
    segment = jnp.sum((places[:, None] >= seg_offsets[None, :]).astype(jnp.int32), axis=1) - 1
    clipped = jnp.maximum(segment, 0).astype(jnp.int32)
    within = places - seg_offsets[clipped]
    is_audio = (segment >= 0) & (within < seg_lengths[clipped])
    source = jnp.where(is_audio, seg_start[clipped] + within, 0).astype(jnp.int32)
    return jnp.where(is_audio[:, None], audio[source], text_embed)


def mix_conv(x_raw, tap_weights):
    row_count = x_raw.shape[0]
    padded = jnp.concatenate([jnp.zeros((3, x_raw.shape[1]), x_raw.dtype), x_raw], axis=0)
    summed = jnp.zeros(x_raw.shape, jnp.float32)
    for offset in range(4):
        summed = summed + padded[offset:offset + row_count].astype(jnp.float32) * tap_weights[offset]
    return jax.nn.silu(summed).astype(jnp.bfloat16)


def run_mixer(group_data):
    x_raw, tap_weights, b_rows, c_rows, step_rows, rate_logs, skips = group_data
    xconv = mix_conv(x_raw, tap_weights)
    head_count = step_rows.shape[0]
    blocks = SEQ_LEN // SPAN
    plain = xconv.reshape(blocks, SPAN, head_count, HDIM)
    b_all = b_rows.reshape(blocks, SPAN, STATE)
    c_all = c_rows.reshape(blocks, SPAN, STATE)
    step_sizes = step_rows.T.reshape(blocks, SPAN, head_count)
    rates = jnp.exp(rate_logs)
    lower_mask = (jnp.arange(SPAN)[:, None] >= jnp.arange(SPAN)[None, :])[:, :, None]

    def advance(state_now, block_data):
        plain_block, b_block, c_block, step_block = block_data
        value = plain_block.astype(jnp.float32)
        b_wide = b_block.astype(jnp.float32)
        c_wide = c_block.astype(jnp.float32)
        log_decay = -step_block * rates[None, :]
        running = jnp.cumsum(log_decay, axis=0)
        gap_logs = running[:, None, :] - running[None, :, :]
        decay_table = jnp.where(lower_mask, jnp.exp(jnp.where(lower_mask, gap_logs, 0.0)), 0.0)
        intersection = jnp.dot(c_block, b_block.T, preferred_element_type=jnp.float32)
        weight = (decay_table * intersection[:, :, None] * step_block[None, :, :]).astype(jnp.bfloat16)
        weight = lax.optimization_barrier(weight).astype(jnp.float32)
        inner_part = jnp.einsum("ijh,jhp->ihp", weight, value, precision=highest)
        inputs = value * step_block[:, :, None]
        carried = jnp.einsum("in,hpn->ihp", c_wide, state_now, precision=high_mode) * jnp.exp(running)[:, :, None]
        output = inner_part + carried + skips[None, :, None] * value
        tail_decay = jnp.exp(running[-1][None, :] - running)
        new_state = state_now * jnp.exp(running[-1])[:, None, None] + jnp.einsum(
            "jhp,jn->hpn", inputs * tail_decay[:, :, None], b_wide, precision=high_mode)
        return new_state, output

    initial = jnp.zeros((head_count, HDIM, STATE), jnp.float32)
    final_state, outputs = lax.scan(advance, initial, (plain, b_all, c_all, step_sizes))
    return outputs.reshape(SEQ_LEN, head_count * HDIM).astype(jnp.bfloat16)


def reference(mel_frames, conv_weight, conv_bias, projector, seg_offsets, seg_lengths, text_embed, mix_taps, input_map, output_map, step_size, decay_log, skip_gain):
    features = front_end(mel_frames, conv_weight, conv_bias, seg_lengths)
    audio = jnp.dot(features, projector.reshape(ENC_W, INNER), preferred_element_type=jnp.float32).astype(jnp.bfloat16)
    x_raw = place_tokens(audio, text_embed, seg_offsets, seg_lengths)
    group_width = INNER // GROUPS
    heads_group = HEADS // GROUPS
    grouped = (
        x_raw.reshape(SEQ_LEN, GROUPS, group_width).transpose(1, 0, 2),
        mix_taps.reshape(4, GROUPS, group_width).transpose(1, 0, 2),
        input_map.reshape(SEQ_LEN, GROUPS, STATE).transpose(1, 0, 2),
        output_map.reshape(SEQ_LEN, GROUPS, STATE).transpose(1, 0, 2),
        step_size.reshape(GROUPS, heads_group, SEQ_LEN),
        decay_log.reshape(GROUPS, heads_group),
        skip_gain.reshape(GROUPS, heads_group),
    )
    mixed = lax.map(run_mixer, grouped)
    return mixed.transpose(1, 0, 2).reshape(SEQ_LEN, INNER)
```

```python
import jax
import jax.numpy as jnp
from jax import lax
from jax.sharding import PartitionSpec as P

HDIM = 64
SPAN = 128
DRIFT = 256


highest = lax.Precision.HIGHEST
high_mode = lax.Precision.HIGH


def from_behind(value, axis, by):
    count = lax.axis_size(axis)
    pairs = [(i, i + by) for i in range(count) if 0 <= i + by < count]
    return lax.ppermute(value, axis, pairs)


def padded_2(block, sides, width):
    for axis, dim in sides:
        count = lax.axis_size(axis)
        forward = [(i, i + 1) for i in range(count - 1)]
        backward = [(target, source) for source, target in forward]
        low = lax.ppermute(
            lax.slice_in_dim(block, block.shape[dim] - width, None, axis=dim), axis, forward
        )
        high = lax.ppermute(lax.slice_in_dim(block, 0, width, axis=dim), axis, backward)
        block = jnp.concatenate([low, block, high], axis=dim)
    return block


def prefix_windows(total, axis):
    count = lax.axis_size(axis)
    first = [d for d in (1, 2) if d < count]
    window = jnp.zeros_like(total)
    for d in first:
        window = window + from_behind(total, axis, d)
    spans = []
    width = len(first)
    while width < count:
        spans.append((width, window))
        window = window + from_behind(window, axis, width)
        width *= 2
    return first, spans


def prefix_state(total, state, first, spans, axis):
    incoming = jnp.zeros_like(state)
    for d in first:
        shifted = from_behind(state.astype(jnp.bfloat16), axis, d).astype(state.dtype)
        if d == 2:
            shifted = shifted * jnp.exp(from_behind(total, axis, 1))[:, None, None]
        incoming = incoming + shifted
    for width, window in spans:
        earlier = from_behind(incoming.astype(jnp.bfloat16), axis, width).astype(state.dtype)
        incoming = earlier * jnp.exp(window)[:, None, None] + incoming
    return incoming


def shards(
    mel_frames,
    conv_weight,
    conv_bias,
    projector,
    seg_offsets,
    seg_lengths,
    text_embed,
    mix_taps,
    input_map,
    output_map,
    step_size,
    decay_log,
    skip_gain,
):
    tiles = mel_frames.shape[0] // 2
    channels = mel_frames.shape[1]
    enc_count = lax.axis_size("enc")
    tile_first = (lax.axis_index("seq") * enc_count + lax.axis_index("enc")) * tiles
    seg_start = jnp.cumsum(seg_lengths) - seg_lengths
    frame_pairs = mel_frames.reshape(tiles, 2 * channels)
    edge_frame = from_behind(frame_pairs[-1:, channels:], ("seq", "enc"), 1)
    tokens = tile_first + jnp.arange(tiles, dtype=jnp.int32)
    opening = jnp.any(tokens[:, None] == seg_start[None, :], axis=1)
    left_frames = jnp.concatenate([edge_frame, frame_pairs[:-1, channels:]], axis=0)
    left_frames = jnp.where(opening[:, None], jnp.zeros_like(left_frames), left_frames)
    stacked = jnp.concatenate([left_frames, frame_pairs], axis=1)
    summed = jnp.dot(stacked, conv_weight, preferred_element_type=jnp.float32) + conv_bias
    features = jax.nn.gelu(summed, approximate=False).astype(jnp.bfloat16)
    column_width = projector.shape[2]
    projected = jnp.dot(
        features, projector.reshape(projector.shape[0], -1), preferred_element_type=jnp.float32
    )
    projected = projected.astype(jnp.bfloat16).reshape(tiles, enc_count, column_width)
    audio_rows = lax.all_to_all(projected, "enc", split_axis=1, concat_axis=0, tiled=True).reshape(
        tiles * enc_count, column_width
    )
    shard_audio = audio_rows.shape[0]
    widened = padded_2(audio_rows, (("seq", 0),), DRIFT)
    row_count = text_embed.shape[0]
    owner_index = lax.axis_index("seq")
    places = owner_index * row_count + jnp.arange(row_count, dtype=jnp.int32)
    segment = jnp.sum((places[:, None] >= seg_offsets[None, :]).astype(jnp.int32), axis=1) - 1
    chosen = jnp.arange(seg_offsets.shape[0], dtype=jnp.int32)[None, :] == segment[:, None]
    offset_here = jnp.sum(jnp.where(chosen, seg_offsets[None, :], 0), axis=1)
    length_here = jnp.sum(jnp.where(chosen, seg_lengths[None, :], 0), axis=1)
    start_here = jnp.sum(jnp.where(chosen, seg_start[None, :], 0), axis=1)
    within = places - offset_here
    is_audio = (segment >= 0) & (within < length_here)
    local_row = jnp.where(is_audio, start_here + within - owner_index * shard_audio + DRIFT, 0)
    x_raw = jnp.where(is_audio[:, None], jnp.take(widened, local_row, axis=0), text_embed)
    previous = from_behind(x_raw[-3:], "seq", 1)
    padded = jnp.concatenate([previous, x_raw], axis=0)
    summed_mix = jnp.zeros(x_raw.shape, jnp.float32)
    for offset in range(4):
        summed_mix = (
            summed_mix + padded[offset : offset + row_count].astype(jnp.float32) * mix_taps[offset]
        )
    mixed_in = jax.nn.silu(summed_mix).astype(jnp.bfloat16)
    head_count = step_size.shape[0]
    blocks = row_count // SPAN
    plain = mixed_in.reshape(blocks, SPAN, head_count, HDIM)
    values = plain.astype(jnp.float32)
    b_rows = input_map.reshape(blocks, SPAN, -1)
    c_rows = output_map.reshape(blocks, SPAN, -1)
    b_all = b_rows.astype(jnp.float32)
    c_all = c_rows.astype(jnp.float32)
    step_sizes = step_size.T.reshape(blocks, SPAN, head_count)
    log_decay = -step_sizes * jnp.exp(decay_log)[None, None, :]
    running = jnp.cumsum(log_decay, axis=1)
    lower_mask = (jnp.arange(SPAN)[:, None] >= jnp.arange(SPAN)[None, :])[None, :, :, None]
    gap_logs = running[:, :, None, :] - running[:, None, :, :]
    decay_table = jnp.where(lower_mask, jnp.exp(jnp.where(lower_mask, gap_logs, 0.0)), 0.0)
    intersection = jnp.einsum("cin,cjn->cij", c_rows, b_rows, preferred_element_type=jnp.float32)
    weight = (decay_table * intersection[..., None] * step_sizes[:, None, :, :]).astype(
        jnp.bfloat16
    )
    inner_part = jnp.einsum("cijh,cjhp->cihp", weight, plain, preferred_element_type=jnp.float32)
    inputs = values * step_sizes[..., None]
    tail_decay = jnp.exp(running[:, -1:, :] - running)
    block_states = jnp.einsum(
        "cjhp,cjn->chpn", inputs * tail_decay[..., None], b_all, precision=high_mode
    )
    totals = running[:, -1, :]
    through = jnp.cumsum(totals, axis=0)
    before_block = through - totals
    block_order = jnp.arange(blocks)
    earlier = (block_order[None, :] < block_order[:, None])[:, :, None]
    weights = jnp.where(
        earlier,
        jnp.exp(jnp.where(earlier, before_block[:, None, :] - through[None, :, :], 0.0)),
        0.0,
    )
    local_starts = jnp.einsum("cdh,dhpn->chpn", weights, block_states, precision=highest)
    device_total = through[-1]
    first, spans = prefix_windows(device_total, "seq")
    device_state = jnp.einsum(
        "dh,dhpn->hpn", jnp.exp(device_total[None, :] - through), block_states, precision=highest
    )

    incoming = prefix_state(device_total, device_state, first, spans, "seq")
    block_in = local_starts + jnp.exp(before_block)[:, :, None, None] * incoming[None]
    carried = (
        jnp.einsum("cin,chpn->cihp", c_all, block_in, precision=high_mode)
        * jnp.exp(running)[..., None]
    )
    output = inner_part + carried + skip_gain[None, None, :, None] * values
    return output.reshape(row_count, head_count * HDIM).astype(jnp.bfloat16)


def solution(mesh):
    return jax.shard_map(
        shards,
        mesh=mesh,
        in_specs=(
            P(("seq", "enc"), None),
            P(),
            P(),
            P(None, None, "head"),
            P(),
            P(),
            P("seq", ("enc", "head")),
            P(None, ("enc", "head")),
            P("seq", "enc"),
            P("seq", "enc"),
            P(("enc", "head"), "seq"),
            P(("enc", "head")),
            P(("enc", "head")),
        ),
        out_specs=P("seq", ("enc", "head")),
        check_vma=False,
    )
```

```python
import jax
import jax.numpy as jnp
from jax import lax
from jax.sharding import PartitionSpec as P

HDIM = 64
SPAN = 128
DRIFT = 256


highest = lax.Precision.HIGHEST
high_mode = lax.Precision.HIGH


def from_behind(value, axis, by):
    count = lax.axis_size(axis)
    pairs = [(i, i + by) for i in range(count) if 0 <= i + by < count]
    return lax.ppermute(value, axis, pairs)


def padded_2(block, sides, width):
    for axis, dim in sides:
        count = lax.axis_size(axis)
        forward = [(i, i + 1) for i in range(count - 1)]
        backward = [(target, source) for source, target in forward]
        low = lax.ppermute(
            lax.slice_in_dim(block, block.shape[dim] - width, None, axis=dim), axis, forward
        )
        high = lax.ppermute(lax.slice_in_dim(block, 0, width, axis=dim), axis, backward)
        block = jnp.concatenate([low, block, high], axis=dim)
    return block


def prefix_state(total, state, axis):
    count = lax.axis_size(axis)
    heads, rows, cols = state.shape

    def pack(t, s):
        column = jnp.broadcast_to(t[:, None, None], (heads, 1, cols))
        return jnp.concatenate([s, column], axis=1)

    def received(t, s, d):
        message = from_behind(pack(t, s), axis, d)
        return message[:, rows, 0], message[:, :rows]

    window = jnp.zeros_like(total)
    incoming = jnp.zeros_like(state)
    width = 0
    if count > 1:
        t_one, s_one = received(total, state, 1)
        window, incoming, width = t_one, s_one, 1
    if count > 2:
        t_two, s_two = received(total, state, 2)
        incoming = s_two * jnp.exp(window)[:, None, None] + incoming
        window = t_two + window
        width = 2
    while 0 < width < count:
        t_far, s_far = received(window, incoming, width)
        incoming = s_far * jnp.exp(window)[:, None, None] + incoming
        window = t_far + window
        width *= 2
    return incoming


def shards(
    mel_frames,
    conv_weight,
    conv_bias,
    projector,
    seg_offsets,
    seg_lengths,
    text_embed,
    mix_taps,
    input_map,
    output_map,
    step_size,
    decay_log,
    skip_gain,
):
    tiles = mel_frames.shape[0] // 2
    channels = mel_frames.shape[1]
    enc_count = lax.axis_size("enc")
    tile_first = (lax.axis_index("seq") * enc_count + lax.axis_index("enc")) * tiles
    seg_start = jnp.cumsum(seg_lengths) - seg_lengths
    frame_pairs = mel_frames.reshape(tiles, 2 * channels)
    edge_frame = from_behind(frame_pairs[-1:, channels:], ("seq", "enc"), 1)
    tokens = tile_first + jnp.arange(tiles, dtype=jnp.int32)
    opening = jnp.any(tokens[:, None] == seg_start[None, :], axis=1)
    left_frames = jnp.concatenate([edge_frame, frame_pairs[:-1, channels:]], axis=0)
    left_frames = jnp.where(opening[:, None], jnp.zeros_like(left_frames), left_frames)
    stacked = jnp.concatenate([left_frames, frame_pairs], axis=1)
    summed = jnp.dot(stacked, conv_weight, preferred_element_type=jnp.float32) + conv_bias
    features = jax.nn.gelu(summed, approximate=False).astype(jnp.bfloat16)
    column_width = projector.shape[2]
    projected = jnp.dot(
        features, projector.reshape(projector.shape[0], -1), preferred_element_type=jnp.float32
    )
    projected = projected.astype(jnp.bfloat16).reshape(tiles, enc_count, column_width)
    audio_rows = lax.all_to_all(projected, "enc", split_axis=1, concat_axis=0, tiled=True).reshape(
        tiles * enc_count, column_width
    )
    shard_audio = audio_rows.shape[0]
    widened = padded_2(audio_rows, (("seq", 0),), DRIFT)
    row_count = text_embed.shape[0]
    owner_index = lax.axis_index("seq")
    places = owner_index * row_count + jnp.arange(row_count, dtype=jnp.int32)
    segment = jnp.sum((places[:, None] >= seg_offsets[None, :]).astype(jnp.int32), axis=1) - 1
    chosen = jnp.arange(seg_offsets.shape[0], dtype=jnp.int32)[None, :] == segment[:, None]
    offset_here = jnp.sum(jnp.where(chosen, seg_offsets[None, :], 0), axis=1)
    length_here = jnp.sum(jnp.where(chosen, seg_lengths[None, :], 0), axis=1)
    start_here = jnp.sum(jnp.where(chosen, seg_start[None, :], 0), axis=1)
    within = places - offset_here
    is_audio = (segment >= 0) & (within < length_here)
    local_row = jnp.where(is_audio, start_here + within - owner_index * shard_audio + DRIFT, 0)
    x_raw = jnp.where(is_audio[:, None], jnp.take(widened, local_row, axis=0), text_embed)
    previous = from_behind(x_raw[-3:], "seq", 1)
    padded = jnp.concatenate([previous, x_raw], axis=0)
    summed_mix = jnp.zeros(x_raw.shape, jnp.float32)
    for offset in range(4):
        summed_mix = (
            summed_mix + padded[offset : offset + row_count].astype(jnp.float32) * mix_taps[offset]
        )
    mixed_in = jax.nn.silu(summed_mix).astype(jnp.bfloat16)
    head_count = step_size.shape[0]
    blocks = row_count // SPAN
    plain = mixed_in.reshape(blocks, SPAN, head_count, HDIM)
    values = plain.astype(jnp.float32)
    b_rows = input_map.reshape(blocks, SPAN, -1)
    c_rows = output_map.reshape(blocks, SPAN, -1)
    b_all = b_rows.astype(jnp.float32)
    c_all = c_rows.astype(jnp.float32)
    step_sizes = step_size.T.reshape(blocks, SPAN, head_count)
    log_decay = -step_sizes * jnp.exp(decay_log)[None, None, :]
    running = jnp.cumsum(log_decay, axis=1)
    lower_mask = (jnp.arange(SPAN)[:, None] >= jnp.arange(SPAN)[None, :])[None, :, :, None]
    gap_logs = running[:, :, None, :] - running[:, None, :, :]
    decay_table = jnp.where(lower_mask, jnp.exp(jnp.where(lower_mask, gap_logs, 0.0)), 0.0)
    intersection = jnp.einsum("cin,cjn->cij", c_rows, b_rows, preferred_element_type=jnp.float32)
    weight = (decay_table * intersection[..., None] * step_sizes[:, None, :, :]).astype(
        jnp.bfloat16
    )
    inner_part = jnp.einsum("cijh,cjhp->cihp", weight, plain, preferred_element_type=jnp.float32)
    inputs = values * step_sizes[..., None]
    tail_decay = jnp.exp(running[:, -1:, :] - running)
    block_states = jnp.einsum(
        "cjhp,cjn->chpn", inputs * tail_decay[..., None], b_all, precision=high_mode
    )
    totals = running[:, -1, :]
    through = jnp.cumsum(totals, axis=0)
    before_block = through - totals
    block_order = jnp.arange(blocks)
    earlier = (block_order[None, :] < block_order[:, None])[:, :, None]
    weights = jnp.where(
        earlier,
        jnp.exp(jnp.where(earlier, before_block[:, None, :] - through[None, :, :], 0.0)),
        0.0,
    )
    local_starts = jnp.einsum("cdh,dhpn->chpn", weights, block_states, precision=highest)
    device_total = through[-1]
    device_state = jnp.einsum(
        "dh,dhpn->hpn", jnp.exp(device_total[None, :] - through), block_states, precision=highest
    )

    incoming = prefix_state(device_total, device_state, "seq")
    block_in = local_starts + jnp.exp(before_block)[:, :, None, None] * incoming[None]
    carried = (
        jnp.einsum("cin,chpn->cihp", c_all, block_in, precision=high_mode)
        * jnp.exp(running)[..., None]
    )
    output = inner_part + carried + skip_gain[None, None, :, None] * values
    return output.reshape(row_count, head_count * HDIM).astype(jnp.bfloat16)


def solution(mesh):
    return jax.shard_map(
        shards,
        mesh=mesh,
        in_specs=(
            P(("seq", "enc"), None),
            P(),
            P(),
            P(None, None, "head"),
            P(),
            P(),
            P("seq", ("enc", "head")),
            P(None, ("enc", "head")),
            P("seq", "enc"),
            P("seq", "enc"),
            P(("enc", "head"), "seq"),
            P(("enc", "head")),
            P(("enc", "head")),
        ),
        out_specs=P("seq", ("enc", "head")),
        check_vma=False,
    )
```

```python
import jax
import jax.numpy as jnp
from jax import lax
from jax.sharding import PartitionSpec as P

HDIM = 64
SPAN = 128
DRIFT = 256


highest = lax.Precision.HIGHEST
high_mode = lax.Precision.HIGH


def from_behind(value, axis, by):
    count = lax.axis_size(axis)
    pairs = [(i, i + by) for i in range(count) if 0 <= i + by < count]
    return lax.ppermute(value, axis, pairs)


def padded_2(block, sides, width):
    for axis, dim in sides:
        count = lax.axis_size(axis)
        forward = [(i, i + 1) for i in range(count - 1)]
        backward = [(target, source) for source, target in forward]
        low = lax.ppermute(
            lax.slice_in_dim(block, block.shape[dim] - width, None, axis=dim), axis, forward
        )
        high = lax.ppermute(lax.slice_in_dim(block, 0, width, axis=dim), axis, backward)
        block = jnp.concatenate([low, block, high], axis=dim)
    return block


def prefix_state(total, state, axis):
    count = lax.axis_size(axis)
    heads, rows, cols = state.shape

    def pack(t, s):
        column = jnp.broadcast_to(t[:, None, None], (heads, 1, cols))
        return jnp.concatenate([s, column], axis=1)

    def received(t, s, d):
        message = from_behind(pack(t, s), axis, d)
        return message[:, rows, 0], message[:, :rows]

    window = jnp.zeros_like(total)
    incoming = jnp.zeros_like(state)
    width = 0
    if count > 1:
        t_one, s_one = received(total, state, 1)
        window, incoming, width = t_one, s_one, 1
    if count > 2:
        t_two, s_two = received(total, state, 2)
        incoming = s_two * jnp.exp(window)[:, None, None] + incoming
        window = t_two + window
        width = 2
    while 0 < width < count:
        t_far, s_far = received(window, incoming, width)
        incoming = s_far * jnp.exp(window)[:, None, None] + incoming
        window = t_far + window
        width *= 2
    return incoming


def shards(
    mel_frames,
    conv_weight,
    conv_bias,
    projector,
    seg_offsets,
    seg_lengths,
    text_embed,
    mix_taps,
    input_map,
    output_map,
    step_size,
    decay_log,
    skip_gain,
):
    tiles = mel_frames.shape[0] // 2
    channels = mel_frames.shape[1]
    enc_count = lax.axis_size("enc")
    seg_start = jnp.cumsum(seg_lengths) - seg_lengths
    frame_pairs = mel_frames.reshape(tiles, 2 * channels)
    owner_pairs = lax.all_gather(frame_pairs, "enc", axis=0, tiled=True)
    shard_audio = owner_pairs.shape[0]
    behind = from_behind(owner_pairs[shard_audio - DRIFT - 1 :], "seq", 1)
    ahead = from_behind(owner_pairs[:DRIFT], "seq", -1)
    wide_pairs = jnp.concatenate([behind, owner_pairs, ahead], axis=0)
    token_count = shard_audio + 2 * DRIFT
    token_first = lax.axis_index("seq") * shard_audio - DRIFT
    tokens = token_first + jnp.arange(token_count, dtype=jnp.int32)
    opening = jnp.any(tokens[:, None] == seg_start[None, :], axis=1)
    left_frames = wide_pairs[:token_count, channels:]
    left_frames = jnp.where(opening[:, None], jnp.zeros_like(left_frames), left_frames)
    stacked = jnp.concatenate([left_frames, wide_pairs[1:]], axis=1)
    summed = jnp.dot(stacked, conv_weight, preferred_element_type=jnp.float32) + conv_bias
    features = jax.nn.gelu(summed, approximate=False).astype(jnp.bfloat16)
    block_columns = lax.dynamic_index_in_dim(projector, lax.axis_index("enc"), 1, False)
    widened = jnp.dot(features, block_columns, preferred_element_type=jnp.float32).astype(
        jnp.bfloat16
    )
    row_count = text_embed.shape[0]
    owner_index = lax.axis_index("seq")
    places = owner_index * row_count + jnp.arange(row_count, dtype=jnp.int32)
    segment = jnp.sum((places[:, None] >= seg_offsets[None, :]).astype(jnp.int32), axis=1) - 1
    chosen = jnp.arange(seg_offsets.shape[0], dtype=jnp.int32)[None, :] == segment[:, None]
    offset_here = jnp.sum(jnp.where(chosen, seg_offsets[None, :], 0), axis=1)
    length_here = jnp.sum(jnp.where(chosen, seg_lengths[None, :], 0), axis=1)
    start_here = jnp.sum(jnp.where(chosen, seg_start[None, :], 0), axis=1)
    within = places - offset_here
    is_audio = (segment >= 0) & (within < length_here)
    local_row = jnp.where(is_audio, start_here + within - owner_index * shard_audio + DRIFT, 0)
    x_raw = jnp.where(is_audio[:, None], jnp.take(widened, local_row, axis=0), text_embed)
    previous = from_behind(x_raw[-3:], "seq", 1)
    padded = jnp.concatenate([previous, x_raw], axis=0)
    summed_mix = jnp.zeros(x_raw.shape, jnp.float32)
    for offset in range(4):
        summed_mix = (
            summed_mix + padded[offset : offset + row_count].astype(jnp.float32) * mix_taps[offset]
        )
    mixed_in = jax.nn.silu(summed_mix).astype(jnp.bfloat16)
    head_count = step_size.shape[0]
    blocks = row_count // SPAN
    plain = mixed_in.reshape(blocks, SPAN, head_count, HDIM)
    values = plain.astype(jnp.float32)
    b_rows = input_map.reshape(blocks, SPAN, -1)
    c_rows = output_map.reshape(blocks, SPAN, -1)
    b_all = b_rows.astype(jnp.float32)
    c_all = c_rows.astype(jnp.float32)
    step_sizes = step_size.T.reshape(blocks, SPAN, head_count)
    log_decay = -step_sizes * jnp.exp(decay_log)[None, None, :]
    running = jnp.cumsum(log_decay, axis=1)
    lower_mask = (jnp.arange(SPAN)[:, None] >= jnp.arange(SPAN)[None, :])[None, :, :, None]
    gap_logs = running[:, :, None, :] - running[:, None, :, :]
    decay_table = jnp.where(lower_mask, jnp.exp(jnp.where(lower_mask, gap_logs, 0.0)), 0.0)
    intersection = jnp.einsum("cin,cjn->cij", c_rows, b_rows, preferred_element_type=jnp.float32)
    weight = (decay_table * intersection[..., None] * step_sizes[:, None, :, :]).astype(
        jnp.bfloat16
    )
    inner_part = jnp.einsum("cijh,cjhp->cihp", weight, plain, preferred_element_type=jnp.float32)
    inputs = values * step_sizes[..., None]
    tail_decay = jnp.exp(running[:, -1:, :] - running)
    block_states = jnp.einsum(
        "cjhp,cjn->chpn", inputs * tail_decay[..., None], b_all, precision=high_mode
    )
    totals = running[:, -1, :]
    through = jnp.cumsum(totals, axis=0)
    before_block = through - totals
    block_order = jnp.arange(blocks)
    earlier = (block_order[None, :] < block_order[:, None])[:, :, None]
    weights = jnp.where(
        earlier,
        jnp.exp(jnp.where(earlier, before_block[:, None, :] - through[None, :, :], 0.0)),
        0.0,
    )
    local_starts = jnp.einsum("cdh,dhpn->chpn", weights, block_states, precision=highest)
    device_total = through[-1]
    device_state = jnp.einsum(
        "dh,dhpn->hpn", jnp.exp(device_total[None, :] - through), block_states, precision=highest
    )

    incoming = prefix_state(device_total, device_state, "seq")
    block_in = local_starts + jnp.exp(before_block)[:, :, None, None] * incoming[None]
    carried = (
        jnp.einsum("cin,chpn->cihp", c_all, block_in, precision=high_mode)
        * jnp.exp(running)[..., None]
    )
    output = inner_part + carried + skip_gain[None, None, :, None] * values
    return output.reshape(row_count, head_count * HDIM).astype(jnp.bfloat16)


def solution(mesh):
    return jax.shard_map(
        shards,
        mesh=mesh,
        in_specs=(
            P(("seq", "enc"), None),
            P(),
            P(),
            P(None, None, "head"),
            P(),
            P(),
            P("seq", ("enc", "head")),
            P(None, ("enc", "head")),
            P("seq", "enc"),
            P("seq", "enc"),
            P(("enc", "head"), "seq"),
            P(("enc", "head")),
            P(("enc", "head")),
        ),
        out_specs=P("seq", ("enc", "head")),
        check_vma=False,
    )
```

```python
import jax
import jax.numpy as jnp
from jax import lax
from jax.sharding import PartitionSpec as P

HDIM = 64
SPAN = 128
DRIFT = 256


highest = lax.Precision.HIGHEST
high_mode = lax.Precision.HIGH


def from_behind(value, axis, by):
    count = lax.axis_size(axis)
    pairs = [(i, i + by) for i in range(count) if 0 <= i + by < count]
    return lax.ppermute(value, axis, pairs)


def padded_2(block, sides, width):
    for axis, dim in sides:
        count = lax.axis_size(axis)
        forward = [(i, i + 1) for i in range(count - 1)]
        backward = [(target, source) for source, target in forward]
        low = lax.ppermute(
            lax.slice_in_dim(block, block.shape[dim] - width, None, axis=dim), axis, forward
        )
        high = lax.ppermute(lax.slice_in_dim(block, 0, width, axis=dim), axis, backward)
        block = jnp.concatenate([low, block, high], axis=dim)
    return block


def prefix_state(total, state, axis):
    count = lax.axis_size(axis)
    heads, rows, cols = state.shape

    def pack(t, s):
        column = jnp.broadcast_to(t[:, None, None], (heads, 1, cols))
        return jnp.concatenate([s, column], axis=1)

    def received(t, s, d):
        message = from_behind(pack(t, s), axis, d)
        return message[:, rows, 0], message[:, :rows]

    window, incoming = total, state
    width = 1
    own = False
    radix = 5
    while width < count:
        radix = min(radix, -(-count // width) + (0 if own else 1))
        parts = [received(window, incoming, m * width) for m in range(radix - 1, 0, -1)]
        if own:
            parts.append((window, incoming))
        window, incoming = parts[0]
        for t_part, s_part in parts[1:]:
            incoming = incoming * jnp.exp(t_part)[:, None, None] + s_part
            window = window + t_part
        width = width * (radix - 1) if not own else width * radix
        own = True
        radix = 4
    if width == 1:
        return jnp.zeros_like(state)
    return incoming


def shards(
    mel_frames,
    conv_weight,
    conv_bias,
    projector,
    seg_offsets,
    seg_lengths,
    text_embed,
    mix_taps,
    input_map,
    output_map,
    step_size,
    decay_log,
    skip_gain,
):
    tiles = mel_frames.shape[0] // 2
    channels = mel_frames.shape[1]
    enc_count = lax.axis_size("enc")
    tile_first = (lax.axis_index("seq") * enc_count + lax.axis_index("enc")) * tiles
    seg_start = jnp.cumsum(seg_lengths) - seg_lengths
    frame_pairs = mel_frames.reshape(tiles, 2 * channels)
    edge_frame = from_behind(frame_pairs[-1:, channels:], ("seq", "enc"), 1)
    tokens = tile_first + jnp.arange(tiles, dtype=jnp.int32)
    opening = jnp.any(tokens[:, None] == seg_start[None, :], axis=1)
    left_frames = jnp.concatenate([edge_frame, frame_pairs[:-1, channels:]], axis=0)
    left_frames = jnp.where(opening[:, None], jnp.zeros_like(left_frames), left_frames)
    stacked = jnp.concatenate([left_frames, frame_pairs], axis=1)
    summed = jnp.dot(stacked, conv_weight, preferred_element_type=jnp.float32) + conv_bias
    features = jax.nn.gelu(summed, approximate=False).astype(jnp.bfloat16)
    column_width = projector.shape[2]
    projected = jnp.dot(
        features, projector.reshape(projector.shape[0], -1), preferred_element_type=jnp.float32
    )
    projected = projected.astype(jnp.bfloat16).reshape(tiles, enc_count, column_width)
    audio_rows = lax.all_to_all(projected, "enc", split_axis=1, concat_axis=0, tiled=True).reshape(
        tiles * enc_count, column_width
    )
    shard_audio = audio_rows.shape[0]
    widened = padded_2(audio_rows, (("seq", 0),), DRIFT)
    row_count = text_embed.shape[0]
    owner_index = lax.axis_index("seq")
    places = owner_index * row_count + jnp.arange(row_count, dtype=jnp.int32)
    segment = jnp.sum((places[:, None] >= seg_offsets[None, :]).astype(jnp.int32), axis=1) - 1
    chosen = jnp.arange(seg_offsets.shape[0], dtype=jnp.int32)[None, :] == segment[:, None]
    offset_here = jnp.sum(jnp.where(chosen, seg_offsets[None, :], 0), axis=1)
    length_here = jnp.sum(jnp.where(chosen, seg_lengths[None, :], 0), axis=1)
    start_here = jnp.sum(jnp.where(chosen, seg_start[None, :], 0), axis=1)
    within = places - offset_here
    is_audio = (segment >= 0) & (within < length_here)
    local_row = jnp.where(is_audio, start_here + within - owner_index * shard_audio + DRIFT, 0)
    x_raw = jnp.where(is_audio[:, None], jnp.take(widened, local_row, axis=0), text_embed)
    previous = from_behind(x_raw[-3:], "seq", 1)
    padded = jnp.concatenate([previous, x_raw], axis=0)
    summed_mix = jnp.zeros(x_raw.shape, jnp.float32)
    for offset in range(4):
        summed_mix = (
            summed_mix + padded[offset : offset + row_count].astype(jnp.float32) * mix_taps[offset]
        )
    mixed_in = jax.nn.silu(summed_mix).astype(jnp.bfloat16)
    head_count = step_size.shape[0]
    blocks = row_count // SPAN
    plain = mixed_in.reshape(blocks, SPAN, head_count, HDIM)
    values = plain.astype(jnp.float32)
    b_rows = input_map.reshape(blocks, SPAN, -1)
    c_rows = output_map.reshape(blocks, SPAN, -1)
    b_all = b_rows.astype(jnp.float32)
    c_all = c_rows.astype(jnp.float32)
    step_sizes = step_size.T.reshape(blocks, SPAN, head_count)
    log_decay = -step_sizes * jnp.exp(decay_log)[None, None, :]
    running = jnp.cumsum(log_decay, axis=1)
    lower_mask = (jnp.arange(SPAN)[:, None] >= jnp.arange(SPAN)[None, :])[None, :, :, None]
    gap_logs = running[:, :, None, :] - running[:, None, :, :]
    decay_table = jnp.where(lower_mask, jnp.exp(jnp.where(lower_mask, gap_logs, 0.0)), 0.0)
    intersection = jnp.einsum("cin,cjn->cij", c_rows, b_rows, preferred_element_type=jnp.float32)
    weight = (decay_table * intersection[..., None] * step_sizes[:, None, :, :]).astype(
        jnp.bfloat16
    )
    inner_part = jnp.einsum("cijh,cjhp->cihp", weight, plain, preferred_element_type=jnp.float32)
    inputs = values * step_sizes[..., None]
    tail_decay = jnp.exp(running[:, -1:, :] - running)
    block_states = jnp.einsum(
        "cjhp,cjn->chpn", inputs * tail_decay[..., None], b_all, precision=high_mode
    )
    totals = running[:, -1, :]
    through = jnp.cumsum(totals, axis=0)
    before_block = through - totals
    block_order = jnp.arange(blocks)
    earlier = (block_order[None, :] < block_order[:, None])[:, :, None]
    weights = jnp.where(
        earlier,
        jnp.exp(jnp.where(earlier, before_block[:, None, :] - through[None, :, :], 0.0)),
        0.0,
    )
    local_starts = jnp.einsum("cdh,dhpn->chpn", weights, block_states, precision=highest)
    device_total = through[-1]
    device_state = jnp.einsum(
        "dh,dhpn->hpn", jnp.exp(device_total[None, :] - through), block_states, precision=highest
    )

    incoming = prefix_state(device_total, device_state, "seq")
    block_in = local_starts + jnp.exp(before_block)[:, :, None, None] * incoming[None]
    carried = (
        jnp.einsum("cin,chpn->cihp", c_all, block_in, precision=high_mode)
        * jnp.exp(running)[..., None]
    )
    output = inner_part + carried + skip_gain[None, None, :, None] * values
    return output.reshape(row_count, head_count * HDIM).astype(jnp.bfloat16)


def solution(mesh):
    return jax.shard_map(
        shards,
        mesh=mesh,
        in_specs=(
            P(("seq", "enc"), None),
            P(),
            P(),
            P(None, None, "head"),
            P(),
            P(),
            P("seq", ("enc", "head")),
            P(None, ("enc", "head")),
            P("seq", "enc"),
            P("seq", "enc"),
            P(("enc", "head"), "seq"),
            P(("enc", "head")),
            P(("enc", "head")),
        ),
        out_specs=P("seq", ("enc", "head")),
        check_vma=False,
    )
```

```python
import jax
import jax.numpy as jnp
from jax import lax
from jax.sharding import PartitionSpec as P

HDIM = 64
SPAN = 128
DRIFT = 256


highest = lax.Precision.HIGHEST
high_mode = lax.Precision.HIGH


def from_behind(value, axis, by):
    count = lax.axis_size(axis)
    pairs = [(i, i + by) for i in range(count) if 0 <= i + by < count]
    return lax.ppermute(value, axis, pairs)


def padded_2(block, sides, width):
    for axis, dim in sides:
        count = lax.axis_size(axis)
        forward = [(i, i + 1) for i in range(count - 1)]
        backward = [(target, source) for source, target in forward]
        low = lax.ppermute(
            lax.slice_in_dim(block, block.shape[dim] - width, None, axis=dim), axis, forward
        )
        high = lax.ppermute(lax.slice_in_dim(block, 0, width, axis=dim), axis, backward)
        block = jnp.concatenate([low, block, high], axis=dim)
    return block


def prefix_windows(total, axis):
    count = lax.axis_size(axis)
    first = [d for d in (1, 2) if d < count]
    window = jnp.zeros_like(total)
    for d in first:
        window = window + from_behind(total, axis, d)
    spans = []
    width = len(first)
    while width < count:
        spans.append((width, window))
        window = window + from_behind(window, axis, width)
        width *= 2
    return first, spans


def prefix_state(total, state, first, spans, axis):
    incoming = jnp.zeros_like(state)
    for d in first:
        shifted = from_behind(state.astype(jnp.bfloat16), axis, d).astype(state.dtype)
        if d == 2:
            shifted = shifted * jnp.exp(from_behind(total, axis, 1))[:, None, None]
        incoming = incoming + shifted
    for width, window in spans:
        earlier = from_behind(incoming.astype(jnp.bfloat16), axis, width).astype(state.dtype)
        incoming = earlier * jnp.exp(window)[:, None, None] + incoming
    return incoming


def shards(
    mel_frames,
    conv_weight,
    conv_bias,
    projector,
    seg_offsets,
    seg_lengths,
    text_embed,
    mix_taps,
    input_map,
    output_map,
    step_size,
    decay_log,
    skip_gain,
):
    tiles = mel_frames.shape[0] // 2
    channels = mel_frames.shape[1]
    enc_count = lax.axis_size("enc")
    tile_first = (lax.axis_index("seq") * enc_count + lax.axis_index("enc")) * tiles
    seg_start = jnp.cumsum(seg_lengths) - seg_lengths
    frame_pairs = mel_frames.reshape(tiles, 2 * channels)
    edge_frame = from_behind(frame_pairs[-1:, channels:], ("seq", "enc"), 1)
    tokens = tile_first + jnp.arange(tiles, dtype=jnp.int32)
    opening = jnp.any(tokens[:, None] == seg_start[None, :], axis=1)
    left_frames = jnp.concatenate([edge_frame, frame_pairs[:-1, channels:]], axis=0)
    left_frames = jnp.where(opening[:, None], jnp.zeros_like(left_frames), left_frames)
    stacked = jnp.concatenate([left_frames, frame_pairs], axis=1)
    summed = jnp.dot(stacked, conv_weight, preferred_element_type=jnp.float32) + conv_bias
    features = jax.nn.gelu(summed, approximate=False).astype(jnp.bfloat16)
    column_width = projector.shape[2]
    projected = jnp.dot(
        features, projector.reshape(projector.shape[0], -1), preferred_element_type=jnp.float32
    )
    projected = projected.astype(jnp.bfloat16).reshape(tiles, enc_count, column_width)
    audio_rows = lax.all_to_all(projected, "enc", split_axis=1, concat_axis=0, tiled=True).reshape(
        tiles * enc_count, column_width
    )
    shard_audio = audio_rows.shape[0]
    extra = 3
    edge = DRIFT + extra
    low_message = jnp.concatenate([audio_rows[shard_audio - edge :], text_embed[-extra:]], axis=0)
    low_received = from_behind(low_message, "seq", 1)
    high = from_behind(audio_rows[:DRIFT], "seq", -1)
    widened = jnp.concatenate([low_received[:edge], audio_rows, high], axis=0)
    text_behind = low_received[edge:]
    row_count = text_embed.shape[0]
    owner_index = lax.axis_index("seq")
    places = owner_index * row_count - extra + jnp.arange(row_count + extra, dtype=jnp.int32)
    segment = jnp.sum((places[:, None] >= seg_offsets[None, :]).astype(jnp.int32), axis=1) - 1
    chosen = jnp.arange(seg_offsets.shape[0], dtype=jnp.int32)[None, :] == segment[:, None]
    offset_here = jnp.sum(jnp.where(chosen, seg_offsets[None, :], 0), axis=1)
    length_here = jnp.sum(jnp.where(chosen, seg_lengths[None, :], 0), axis=1)
    start_here = jnp.sum(jnp.where(chosen, seg_start[None, :], 0), axis=1)
    within = places - offset_here
    is_audio = (segment >= 0) & (within < length_here)
    local_row = jnp.where(is_audio, start_here + within - owner_index * shard_audio + edge, 0)
    text_rows = jnp.concatenate([text_behind, text_embed], axis=0)
    padded = jnp.where(is_audio[:, None], jnp.take(widened, local_row, axis=0), text_rows)
    summed_mix = jnp.zeros((row_count, padded.shape[1]), jnp.float32)
    for offset in range(4):
        summed_mix = (
            summed_mix + padded[offset : offset + row_count].astype(jnp.float32) * mix_taps[offset]
        )
    mixed_in = jax.nn.silu(summed_mix).astype(jnp.bfloat16)
    head_count = step_size.shape[0]
    blocks = row_count // SPAN
    plain = mixed_in.reshape(blocks, SPAN, head_count, HDIM)
    values = plain.astype(jnp.float32)
    b_rows = input_map.reshape(blocks, SPAN, -1)
    c_rows = output_map.reshape(blocks, SPAN, -1)
    b_all = b_rows.astype(jnp.float32)
    c_all = c_rows.astype(jnp.float32)
    step_sizes = step_size.T.reshape(blocks, SPAN, head_count)
    log_decay = -step_sizes * jnp.exp(decay_log)[None, None, :]
    running = jnp.cumsum(log_decay, axis=1)
    lower_mask = (jnp.arange(SPAN)[:, None] >= jnp.arange(SPAN)[None, :])[None, :, :, None]
    gap_logs = running[:, :, None, :] - running[:, None, :, :]
    decay_table = jnp.where(lower_mask, jnp.exp(jnp.where(lower_mask, gap_logs, 0.0)), 0.0)
    intersection = jnp.einsum("cin,cjn->cij", c_rows, b_rows, preferred_element_type=jnp.float32)
    weight = (decay_table * intersection[..., None] * step_sizes[:, None, :, :]).astype(
        jnp.bfloat16
    )
    inner_part = jnp.einsum("cijh,cjhp->cihp", weight, plain, preferred_element_type=jnp.float32)
    inputs = values * step_sizes[..., None]
    tail_decay = jnp.exp(running[:, -1:, :] - running)
    block_states = jnp.einsum(
        "cjhp,cjn->chpn", inputs * tail_decay[..., None], b_all, precision=high_mode
    )
    totals = running[:, -1, :]
    through = jnp.cumsum(totals, axis=0)
    before_block = through - totals
    block_order = jnp.arange(blocks)
    earlier = (block_order[None, :] < block_order[:, None])[:, :, None]
    weights = jnp.where(
        earlier,
        jnp.exp(jnp.where(earlier, before_block[:, None, :] - through[None, :, :], 0.0)),
        0.0,
    )
    local_starts = jnp.einsum("cdh,dhpn->chpn", weights, block_states, precision=highest)
    device_total = through[-1]
    first, spans = prefix_windows(device_total, "seq")
    device_state = jnp.einsum(
        "dh,dhpn->hpn", jnp.exp(device_total[None, :] - through), block_states, precision=highest
    )

    incoming = prefix_state(device_total, device_state, first, spans, "seq")
    block_in = local_starts + jnp.exp(before_block)[:, :, None, None] * incoming[None]
    carried = (
        jnp.einsum("cin,chpn->cihp", c_all, block_in, precision=high_mode)
        * jnp.exp(running)[..., None]
    )
    output = inner_part + carried + skip_gain[None, None, :, None] * values
    return output.reshape(row_count, head_count * HDIM).astype(jnp.bfloat16)


def solution(mesh):
    return jax.shard_map(
        shards,
        mesh=mesh,
        in_specs=(
            P(("seq", "enc"), None),
            P(),
            P(),
            P(None, None, "head"),
            P(),
            P(),
            P("seq", ("enc", "head")),
            P(None, ("enc", "head")),
            P("seq", "enc"),
            P("seq", "enc"),
            P(("enc", "head"), "seq"),
            P(("enc", "head")),
            P(("enc", "head")),
        ),
        out_specs=P("seq", ("enc", "head")),
        check_vma=False,
    )
```

```python
import jax
import jax.numpy as jnp
from jax import lax
from jax.sharding import PartitionSpec as P

HDIM = 64
SPAN = 128
DRIFT = 256


highest = lax.Precision.HIGHEST
high_mode = lax.Precision.HIGH


def from_behind(value, axis, by):
    count = lax.axis_size(axis)
    pairs = [(i, i + by) for i in range(count) if 0 <= i + by < count]
    return lax.ppermute(value, axis, pairs)


def padded_2(block, sides, width):
    for axis, dim in sides:
        count = lax.axis_size(axis)
        forward = [(i, i + 1) for i in range(count - 1)]
        backward = [(target, source) for source, target in forward]
        low = lax.ppermute(
            lax.slice_in_dim(block, block.shape[dim] - width, None, axis=dim), axis, forward
        )
        high = lax.ppermute(lax.slice_in_dim(block, 0, width, axis=dim), axis, backward)
        block = jnp.concatenate([low, block, high], axis=dim)
    return block


def prefix_windows(total, axis):
    count = lax.axis_size(axis)
    first = [d for d in (1, 2) if d < count]
    window = jnp.zeros_like(total)
    for d in first:
        window = window + from_behind(total, axis, d)
    spans = []
    width = len(first)
    while width < count:
        spans.append((width, window))
        window = window + from_behind(window, axis, width)
        width *= 2
    return first, spans


def prefix_state(total, state, first, spans, axis):
    incoming = jnp.zeros_like(state)
    for d in first:
        shifted = from_behind(state.astype(jnp.bfloat16), axis, d).astype(state.dtype)
        if d == 2:
            shifted = shifted * jnp.exp(from_behind(total, axis, 1))[:, None, None]
        incoming = incoming + shifted
    for width, window in spans:
        earlier = from_behind(incoming.astype(jnp.bfloat16), axis, width).astype(state.dtype)
        incoming = earlier * jnp.exp(window)[:, None, None] + incoming
    return incoming


def shards(
    mel_frames,
    conv_weight,
    conv_bias,
    projector,
    seg_offsets,
    seg_lengths,
    text_embed,
    mix_taps,
    input_map,
    output_map,
    step_size,
    decay_log,
    skip_gain,
):
    tiles = mel_frames.shape[0] // 2
    channels = mel_frames.shape[1]
    enc_count = lax.axis_size("enc")
    tile_first = (lax.axis_index("seq") * enc_count + lax.axis_index("enc")) * tiles
    seg_start = jnp.cumsum(seg_lengths) - seg_lengths
    frame_pairs = mel_frames.reshape(tiles, 2 * channels)
    edge_frame = from_behind(frame_pairs[-1:, channels:], ("seq", "enc"), 1)
    tokens = tile_first + jnp.arange(tiles, dtype=jnp.int32)
    opening = jnp.any(tokens[:, None] == seg_start[None, :], axis=1)
    left_frames = jnp.concatenate([edge_frame, frame_pairs[:-1, channels:]], axis=0)
    left_frames = jnp.where(opening[:, None], jnp.zeros_like(left_frames), left_frames)
    stacked = jnp.concatenate([left_frames, frame_pairs], axis=1)
    summed = jnp.dot(stacked, conv_weight, preferred_element_type=jnp.float32) + conv_bias
    features = jax.nn.gelu(summed, approximate=False).astype(jnp.bfloat16)
    column_width = projector.shape[2]
    projected = jnp.einsum(
        "cbk,tc->btk", projector, features, preferred_element_type=jnp.float32
    ).astype(jnp.bfloat16).transpose(1, 0, 2)
    audio_rows = lax.all_to_all(projected, "enc", split_axis=1, concat_axis=0, tiled=True).reshape(
        tiles * enc_count, column_width
    )
    shard_audio = audio_rows.shape[0]
    extra = 3
    edge = DRIFT + extra
    low_message = jnp.concatenate([audio_rows[shard_audio - edge :], text_embed[-extra:]], axis=0)
    low_received = from_behind(low_message, "seq", 1)
    high = from_behind(audio_rows[:DRIFT], "seq", -1)
    widened = jnp.concatenate([low_received[:edge], audio_rows, high], axis=0)
    text_behind = low_received[edge:]
    row_count = text_embed.shape[0]
    owner_index = lax.axis_index("seq")
    places = owner_index * row_count - extra + jnp.arange(row_count + extra, dtype=jnp.int32)
    segment = jnp.sum((places[:, None] >= seg_offsets[None, :]).astype(jnp.int32), axis=1) - 1
    chosen = jnp.arange(seg_offsets.shape[0], dtype=jnp.int32)[None, :] == segment[:, None]
    offset_here = jnp.sum(jnp.where(chosen, seg_offsets[None, :], 0), axis=1)
    length_here = jnp.sum(jnp.where(chosen, seg_lengths[None, :], 0), axis=1)
    start_here = jnp.sum(jnp.where(chosen, seg_start[None, :], 0), axis=1)
    within = places - offset_here
    is_audio = (segment >= 0) & (within < length_here)
    local_row = jnp.where(is_audio, start_here + within - owner_index * shard_audio + edge, 0)
    text_rows = jnp.concatenate([text_behind, text_embed], axis=0)
    padded = jnp.where(is_audio[:, None], jnp.take(widened, local_row, axis=0), text_rows)
    summed_mix = jnp.zeros((row_count, padded.shape[1]), jnp.float32)
    for offset in range(4):
        summed_mix = (
            summed_mix + padded[offset : offset + row_count].astype(jnp.float32) * mix_taps[offset]
        )
    mixed_in = jax.nn.silu(summed_mix).astype(jnp.bfloat16)
    head_count = step_size.shape[0]
    blocks = row_count // SPAN
    plain = mixed_in.reshape(blocks, SPAN, head_count, HDIM)
    values = plain.astype(jnp.float32)
    b_rows = input_map.reshape(blocks, SPAN, -1)
    c_rows = output_map.reshape(blocks, SPAN, -1)
    b_all = b_rows.astype(jnp.float32)
    c_all = c_rows.astype(jnp.float32)
    step_sizes = step_size.T.reshape(blocks, SPAN, head_count)
    log_decay = -step_sizes * jnp.exp(decay_log)[None, None, :]
    running = jnp.cumsum(log_decay, axis=1)
    lower_mask = (jnp.arange(SPAN)[:, None] >= jnp.arange(SPAN)[None, :])[None, :, :, None]
    gap_logs = running[:, :, None, :] - running[:, None, :, :]
    decay_table = jnp.where(lower_mask, jnp.exp(jnp.where(lower_mask, gap_logs, 0.0)), 0.0)
    intersection = jnp.einsum("cin,cjn->cij", c_rows, b_rows, preferred_element_type=jnp.float32)
    weight = (decay_table * intersection[..., None] * step_sizes[:, None, :, :]).astype(
        jnp.bfloat16
    )
    inner_part = jnp.einsum("cijh,cjhp->cihp", weight, plain, preferred_element_type=jnp.float32)
    inputs = values * step_sizes[..., None]
    tail_decay = jnp.exp(running[:, -1:, :] - running)
    block_states = jnp.einsum(
        "cjhp,cjn->chpn", inputs * tail_decay[..., None], b_all, precision=high_mode
    )
    totals = running[:, -1, :]
    through = jnp.cumsum(totals, axis=0)
    before_block = through - totals
    block_order = jnp.arange(blocks)
    earlier = (block_order[None, :] < block_order[:, None])[:, :, None]
    weights = jnp.where(
        earlier,
        jnp.exp(jnp.where(earlier, before_block[:, None, :] - through[None, :, :], 0.0)),
        0.0,
    )
    local_starts = jnp.einsum("cdh,dhpn->chpn", weights, block_states, precision=highest)
    device_total = through[-1]
    first, spans = prefix_windows(device_total, "seq")
    device_state = jnp.einsum(
        "dh,dhpn->hpn", jnp.exp(device_total[None, :] - through), block_states, precision=highest
    )

    incoming = prefix_state(device_total, device_state, first, spans, "seq")
    block_in = local_starts + jnp.exp(before_block)[:, :, None, None] * incoming[None]
    carried = (
        jnp.einsum("cin,chpn->cihp", c_all, block_in, precision=high_mode)
        * jnp.exp(running)[..., None]
    )
    output = inner_part + carried + skip_gain[None, None, :, None] * values
    return output.reshape(row_count, head_count * HDIM).astype(jnp.bfloat16)


def solution(mesh):
    return jax.shard_map(
        shards,
        mesh=mesh,
        in_specs=(
            P(("seq", "enc"), None),
            P(),
            P(),
            P(None, None, "head"),
            P(),
            P(),
            P("seq", ("enc", "head")),
            P(None, ("enc", "head")),
            P("seq", "enc"),
            P("seq", "enc"),
            P(("enc", "head"), "seq"),
            P(("enc", "head")),
            P(("enc", "head")),
        ),
        out_specs=P("seq", ("enc", "head")),
        check_vma=False,
    )
```

```python
import jax
import jax.numpy as jnp
from jax import lax
from jax.sharding import PartitionSpec as P

HDIM = 64
SPAN = 128
DRIFT = 256


highest = lax.Precision.HIGHEST
high_mode = lax.Precision.HIGH


def from_behind(value, axis, by):
    count = lax.axis_size(axis)
    pairs = [(i, i + by) for i in range(count) if 0 <= i + by < count]
    return lax.ppermute(value, axis, pairs)


def padded_2(block, sides, width):
    for axis, dim in sides:
        count = lax.axis_size(axis)
        forward = [(i, i + 1) for i in range(count - 1)]
        backward = [(target, source) for source, target in forward]
        low = lax.ppermute(
            lax.slice_in_dim(block, block.shape[dim] - width, None, axis=dim), axis, forward
        )
        high = lax.ppermute(lax.slice_in_dim(block, 0, width, axis=dim), axis, backward)
        block = jnp.concatenate([low, block, high], axis=dim)
    return block


def prefix_windows(total, axis):
    count = lax.axis_size(axis)
    first = [d for d in (1, 2) if d < count]
    window = jnp.zeros_like(total)
    for d in first:
        window = window + from_behind(total, axis, d)
    spans = []
    width = len(first)
    while width < count:
        spans.append((width, window))
        window = window + from_behind(window, axis, width)
        width *= 2
    return first, spans


def prefix_state(total, state, first, spans, axis):
    incoming = jnp.zeros_like(state)
    for d in first:
        shifted = from_behind(state.astype(jnp.bfloat16), axis, d).astype(state.dtype)
        if d == 2:
            shifted = shifted * jnp.exp(from_behind(total, axis, 1))[:, None, None]
        incoming = incoming + shifted
    for width, window in spans:
        earlier = from_behind(incoming.astype(jnp.bfloat16), axis, width).astype(state.dtype)
        incoming = earlier * jnp.exp(window)[:, None, None] + incoming
    return incoming


def shards(
    mel_frames,
    conv_weight,
    conv_bias,
    projector,
    seg_offsets,
    seg_lengths,
    text_embed,
    mix_taps,
    input_map,
    output_map,
    step_size,
    decay_log,
    skip_gain,
):
    tiles = mel_frames.shape[0] // 2
    channels = mel_frames.shape[1]
    enc_count = lax.axis_size("enc")
    tile_first = (lax.axis_index("seq") * enc_count + lax.axis_index("enc")) * tiles
    seg_start = jnp.cumsum(seg_lengths) - seg_lengths
    frame_pairs = mel_frames.reshape(tiles, 2 * channels)
    edge_frame = from_behind(frame_pairs[-1:, channels:], ("seq", "enc"), 1)
    tokens = tile_first + jnp.arange(tiles, dtype=jnp.int32)
    opening = jnp.any(tokens[:, None] == seg_start[None, :], axis=1)
    left_frames = jnp.concatenate([edge_frame, frame_pairs[:-1, channels:]], axis=0)
    left_frames = jnp.where(opening[:, None], jnp.zeros_like(left_frames), left_frames)
    stacked = jnp.concatenate([left_frames, frame_pairs], axis=1)
    summed = jnp.dot(stacked, conv_weight, preferred_element_type=jnp.float32) + conv_bias
    features = jax.nn.gelu(summed, approximate=False).astype(jnp.bfloat16)
    column_width = projector.shape[2]
    projected = jnp.einsum(
        "cbk,tc->btk", projector, features, preferred_element_type=jnp.float32
    ).astype(jnp.bfloat16).transpose(1, 0, 2)
    audio_rows = lax.all_to_all(projected, "enc", split_axis=1, concat_axis=0, tiled=True).reshape(
        tiles * enc_count, column_width
    )
    shard_audio = audio_rows.shape[0]
    extra = 3
    edge = DRIFT + extra
    low_message = jnp.concatenate([audio_rows[shard_audio - edge :], text_embed[-extra:]], axis=0)
    low_received = from_behind(low_message, "seq", 1)
    high = from_behind(audio_rows[:DRIFT], "seq", -1)
    widened = jnp.concatenate([low_received[:edge], audio_rows, high], axis=0)
    text_behind = low_received[edge:]
    row_count = text_embed.shape[0]
    owner_index = lax.axis_index("seq")
    places = owner_index * row_count - extra + jnp.arange(row_count + extra, dtype=jnp.int32)
    segment = jnp.sum((places[:, None] >= seg_offsets[None, :]).astype(jnp.int32), axis=1) - 1
    chosen = jnp.arange(seg_offsets.shape[0], dtype=jnp.int32)[None, :] == segment[:, None]
    offset_here = jnp.sum(jnp.where(chosen, seg_offsets[None, :], 0), axis=1)
    length_here = jnp.sum(jnp.where(chosen, seg_lengths[None, :], 0), axis=1)
    start_here = jnp.sum(jnp.where(chosen, seg_start[None, :], 0), axis=1)
    within = places - offset_here
    is_audio = (segment >= 0) & (within < length_here)
    local_row = jnp.where(is_audio, start_here + within - owner_index * shard_audio + edge, 0)
    text_rows = jnp.concatenate([text_behind, text_embed], axis=0)
    padded = jnp.where(is_audio[:, None], jnp.take(widened, local_row, axis=0), text_rows)
    summed_mix = jnp.zeros((row_count, padded.shape[1]), jnp.float32)
    for offset in range(4):
        summed_mix = (
            summed_mix + padded[offset : offset + row_count].astype(jnp.float32) * mix_taps[offset]
        )
    mixed_in = jax.nn.silu(summed_mix).astype(jnp.bfloat16)
    head_count = step_size.shape[0]
    blocks = row_count // SPAN
    width = head_count * HDIM
    plain = mixed_in.reshape(blocks, SPAN, width)
    values = plain.astype(jnp.float32)
    b_rows = input_map.reshape(blocks, SPAN, -1)
    c_rows = output_map.reshape(blocks, SPAN, -1)
    b_all = b_rows.astype(jnp.float32)
    c_all = c_rows.astype(jnp.float32)
    column_head = jnp.arange(width, dtype=jnp.int32) // HDIM

    def spread(per_head):
        return jnp.repeat(per_head, HDIM, axis=-1)

    step_sizes = step_size.T.reshape(blocks, SPAN, head_count)
    log_decay = -step_sizes * jnp.exp(decay_log)[None, None, :]
    running = jnp.cumsum(log_decay, axis=1)
    lower_mask = (jnp.arange(SPAN)[:, None] >= jnp.arange(SPAN)[None, :])[None, :, :, None]
    gap_logs = running[:, :, None, :] - running[:, None, :, :]
    decay_table = jnp.where(lower_mask, jnp.exp(jnp.where(lower_mask, gap_logs, 0.0)), 0.0)
    intersection = jnp.einsum("cin,cjn->cij", c_rows, b_rows, preferred_element_type=jnp.float32)
    weight = (decay_table * intersection[..., None] * step_sizes[:, None, :, :]).astype(
        jnp.bfloat16
    )
    inner_part = jnp.zeros(values.shape, jnp.float32)
    for head in range(head_count):
        per_head = jnp.einsum(
            "cij,cjw->ciw", weight[..., head], plain, preferred_element_type=jnp.float32
        )
        inner_part = jnp.where(column_head == head, per_head, inner_part)
    inputs = values * spread(step_sizes)
    tail_decay = jnp.exp(running[:, -1:, :] - running)
    block_states = jnp.einsum(
        "cjw,cjn->cwn", inputs * spread(tail_decay), b_all, precision=high_mode
    )
    totals = running[:, -1, :]
    through = jnp.cumsum(totals, axis=0)
    before_block = through - totals
    block_order = jnp.arange(blocks)
    earlier = (block_order[None, :] < block_order[:, None])[:, :, None]
    weights = jnp.where(
        earlier,
        jnp.exp(jnp.where(earlier, before_block[:, None, :] - through[None, :, :], 0.0)),
        0.0,
    )
    local_starts = jnp.einsum("cdw,dwn->cwn", spread(weights), block_states, precision=highest)
    device_total = through[-1]
    device_state = jnp.einsum(
        "dw,dwn->wn", spread(jnp.exp(device_total[None, :] - through)), block_states,
        precision=highest,
    )
    first, spans = prefix_windows(device_total, "seq")
    incoming = prefix_state(
        device_total, device_state.reshape(head_count, HDIM, -1), first, spans, "seq"
    ).reshape(width, -1)
    block_in = local_starts + spread(jnp.exp(before_block))[:, :, None] * incoming[None]
    carried = (
        jnp.einsum("cin,cwn->ciw", c_all, block_in, precision=high_mode)
        * spread(jnp.exp(running))
    )
    output = inner_part + carried + spread(skip_gain)[None, None, :] * values
    return output.reshape(row_count, width).astype(jnp.bfloat16)


def solution(mesh):
    return jax.shard_map(
        shards,
        mesh=mesh,
        in_specs=(
            P(("seq", "enc"), None),
            P(),
            P(),
            P(None, None, "head"),
            P(),
            P(),
            P("seq", ("enc", "head")),
            P(None, ("enc", "head")),
            P("seq", "enc"),
            P("seq", "enc"),
            P(("enc", "head"), "seq"),
            P(("enc", "head")),
            P(("enc", "head")),
        ),
        out_specs=P("seq", ("enc", "head")),
        check_vma=False,
    )
```

```python
import jax
import jax.numpy as jnp
from jax import lax
from jax.sharding import PartitionSpec as P

HDIM = 64
SPAN = 128
DRIFT = 256


highest = lax.Precision.HIGHEST
high_mode = lax.Precision.HIGH


def from_behind(value, axis, by):
    count = lax.axis_size(axis)
    pairs = [(i, i + by) for i in range(count) if 0 <= i + by < count]
    return lax.ppermute(value, axis, pairs)


def padded_2(block, sides, width):
    for axis, dim in sides:
        count = lax.axis_size(axis)
        forward = [(i, i + 1) for i in range(count - 1)]
        backward = [(target, source) for source, target in forward]
        low = lax.ppermute(
            lax.slice_in_dim(block, block.shape[dim] - width, None, axis=dim), axis, forward
        )
        high = lax.ppermute(lax.slice_in_dim(block, 0, width, axis=dim), axis, backward)
        block = jnp.concatenate([low, block, high], axis=dim)
    return block


def prefix_windows(total, axis):
    count = lax.axis_size(axis)
    first = [d for d in (1, 2) if d < count]
    window = jnp.zeros_like(total)
    for d in first:
        window = window + from_behind(total, axis, d)
    spans = []
    width = len(first)
    while width < count:
        spans.append((width, window))
        window = window + from_behind(window, axis, width)
        width *= 2
    return first, spans


def prefix_state(total, state, first, spans, axis):
    incoming = jnp.zeros_like(state)
    for d in first:
        shifted = from_behind(state.astype(jnp.bfloat16), axis, d).astype(state.dtype)
        if d == 2:
            shifted = shifted * jnp.exp(from_behind(total, axis, 1))[:, None, None]
        incoming = incoming + shifted
    for width, window in spans:
        earlier = from_behind(incoming.astype(jnp.bfloat16), axis, width).astype(state.dtype)
        incoming = earlier * jnp.exp(window)[:, None, None] + incoming
    return incoming


def shards(
    mel_frames,
    conv_weight,
    conv_bias,
    projector,
    seg_offsets,
    seg_lengths,
    text_embed,
    mix_taps,
    input_map,
    output_map,
    step_size,
    decay_log,
    skip_gain,
):
    head_count = step_size.shape[0]
    blocks = text_embed.shape[0] // SPAN
    step_sizes = step_size.T.reshape(blocks, SPAN, head_count)
    log_decay = -step_sizes * jnp.exp(decay_log)[None, None, :]
    running = jnp.cumsum(log_decay, axis=1)
    totals = running[:, -1, :]
    through = jnp.cumsum(totals, axis=0)
    device_total = through[-1]
    first, spans = prefix_windows(device_total, "seq")
    mel_frames, windows = lax.optimization_barrier((mel_frames, [w for _, w in spans]))
    spans = [(width, w) for (width, _), w in zip(spans, windows)]
    tiles = mel_frames.shape[0] // 2
    channels = mel_frames.shape[1]
    enc_count = lax.axis_size("enc")
    tile_first = (lax.axis_index("seq") * enc_count + lax.axis_index("enc")) * tiles
    seg_start = jnp.cumsum(seg_lengths) - seg_lengths
    frame_pairs = mel_frames.reshape(tiles, 2 * channels)
    edge_frame = from_behind(frame_pairs[-1:, channels:], ("seq", "enc"), 1)
    tokens = tile_first + jnp.arange(tiles, dtype=jnp.int32)
    opening = jnp.any(tokens[:, None] == seg_start[None, :], axis=1)
    left_frames = jnp.concatenate([edge_frame, frame_pairs[:-1, channels:]], axis=0)
    left_frames = jnp.where(opening[:, None], jnp.zeros_like(left_frames), left_frames)
    stacked = jnp.concatenate([left_frames, frame_pairs], axis=1)
    summed = jnp.dot(stacked, conv_weight, preferred_element_type=jnp.float32) + conv_bias
    features = jax.nn.gelu(summed, approximate=False).astype(jnp.bfloat16)
    column_width = projector.shape[2]
    projected = jnp.einsum(
        "cbk,tc->btk", projector, features, preferred_element_type=jnp.float32
    ).astype(jnp.bfloat16).transpose(1, 0, 2)
    audio_rows = lax.all_to_all(projected, "enc", split_axis=1, concat_axis=0, tiled=True).reshape(
        tiles * enc_count, column_width
    )
    shard_audio = audio_rows.shape[0]
    extra = 3
    edge = DRIFT + extra
    low_message = jnp.concatenate([audio_rows[shard_audio - edge :], text_embed[-extra:]], axis=0)
    low_received = from_behind(low_message, "seq", 1)
    high = from_behind(audio_rows[:DRIFT], "seq", -1)
    widened = jnp.concatenate([low_received[:edge], audio_rows, high], axis=0)
    text_behind = low_received[edge:]
    row_count = text_embed.shape[0]
    owner_index = lax.axis_index("seq")
    places = owner_index * row_count - extra + jnp.arange(row_count + extra, dtype=jnp.int32)
    segment = jnp.sum((places[:, None] >= seg_offsets[None, :]).astype(jnp.int32), axis=1) - 1
    chosen = jnp.arange(seg_offsets.shape[0], dtype=jnp.int32)[None, :] == segment[:, None]
    offset_here = jnp.sum(jnp.where(chosen, seg_offsets[None, :], 0), axis=1)
    length_here = jnp.sum(jnp.where(chosen, seg_lengths[None, :], 0), axis=1)
    start_here = jnp.sum(jnp.where(chosen, seg_start[None, :], 0), axis=1)
    within = places - offset_here
    is_audio = (segment >= 0) & (within < length_here)
    local_row = jnp.where(is_audio, start_here + within - owner_index * shard_audio + edge, 0)
    text_rows = jnp.concatenate([text_behind, text_embed], axis=0)
    padded = jnp.where(is_audio[:, None], jnp.take(widened, local_row, axis=0), text_rows)
    summed_mix = jnp.zeros((row_count, padded.shape[1]), jnp.float32)
    for offset in range(4):
        summed_mix = (
            summed_mix + padded[offset : offset + row_count].astype(jnp.float32) * mix_taps[offset]
        )
    mixed_in = jax.nn.silu(summed_mix).astype(jnp.bfloat16)
    width = head_count * HDIM
    plain = mixed_in.reshape(blocks, SPAN, width)
    values = plain.astype(jnp.float32)
    b_rows = input_map.reshape(blocks, SPAN, -1)
    c_rows = output_map.reshape(blocks, SPAN, -1)
    b_all = b_rows.astype(jnp.float32)
    c_all = c_rows.astype(jnp.float32)
    column_head = jnp.arange(width, dtype=jnp.int32) // HDIM

    def spread(per_head):
        return jnp.repeat(per_head, HDIM, axis=-1)

    lower_mask = (jnp.arange(SPAN)[:, None] >= jnp.arange(SPAN)[None, :])[None, :, :, None]
    gap_logs = running[:, :, None, :] - running[:, None, :, :]
    decay_table = jnp.where(lower_mask, jnp.exp(jnp.where(lower_mask, gap_logs, 0.0)), 0.0)
    intersection = jnp.einsum("cin,cjn->cij", c_rows, b_rows, preferred_element_type=jnp.float32)
    weight = (decay_table * intersection[..., None] * step_sizes[:, None, :, :]).astype(
        jnp.bfloat16
    )
    inner_part = jnp.zeros(values.shape, jnp.float32)
    for head in range(head_count):
        per_head = jnp.einsum(
            "cij,cjw->ciw", weight[..., head], plain, preferred_element_type=jnp.float32
        )
        inner_part = jnp.where(column_head == head, per_head, inner_part)
    inputs = values * spread(step_sizes)
    tail_decay = jnp.exp(running[:, -1:, :] - running)
    block_states = jnp.einsum(
        "cjw,cjn->cwn", inputs * spread(tail_decay), b_all, precision=high_mode
    )
    before_block = through - totals
    block_order = jnp.arange(blocks)
    earlier = (block_order[None, :] < block_order[:, None])[:, :, None]
    weights = jnp.where(
        earlier,
        jnp.exp(jnp.where(earlier, before_block[:, None, :] - through[None, :, :], 0.0)),
        0.0,
    )
    local_starts = jnp.einsum("cdw,dwn->cwn", spread(weights), block_states, precision=highest)
    device_state = jnp.einsum(
        "dw,dwn->wn", spread(jnp.exp(device_total[None, :] - through)), block_states,
        precision=highest,
    )
    incoming = prefix_state(
        device_total, device_state.reshape(head_count, HDIM, -1), first, spans, "seq"
    ).reshape(width, -1)
    block_in = local_starts + spread(jnp.exp(before_block))[:, :, None] * incoming[None]
    carried = (
        jnp.einsum("cin,cwn->ciw", c_all, block_in, precision=high_mode)
        * spread(jnp.exp(running))
    )
    output = inner_part + carried + spread(skip_gain)[None, None, :] * values
    return output.reshape(row_count, width).astype(jnp.bfloat16)


def solution(mesh):
    return jax.shard_map(
        shards,
        mesh=mesh,
        in_specs=(
            P(("seq", "enc"), None),
            P(),
            P(),
            P(None, None, "head"),
            P(),
            P(),
            P("seq", ("enc", "head")),
            P(None, ("enc", "head")),
            P("seq", "enc"),
            P("seq", "enc"),
            P(("enc", "head"), "seq"),
            P(("enc", "head")),
            P(("enc", "head")),
        ),
        out_specs=P("seq", ("enc", "head")),
        check_vma=False,
    )
```
